128 devices in a mesh: tok: 16 (over x, y), wid: 8 (over z, core).
Axes of the slice: x: 4, y: 4, z: 4, core: 2. Of those that a mesh axis runs over, the one named last changes fastest.
Arguments:
- patches: bfloat16 [1536, 8, 6144], P('tok', None, 'wid'), may hold values from -6 to 6
- w_query: bfloat16 [6144, 4096], P('tok', 'wid'), may hold values from -0.102062073 to 0.102062073
- w_key: bfloat16 [6144, 4096], P('tok', 'wid'), may hold values from -0.102062073 to 0.102062073
- w_value: bfloat16 [6144, 4096], P('tok', 'wid'), may hold values from -0.078125 to 0.078125
- q_gain: float32 [4096], P('wid'), may hold values from 0.5 to 6
- k_gain: float32 [4096], P('wid'), may hold values from 0.5 to 6
- w_out: bfloat16 [4096, 6144], P('tok', 'wid'), may hold values from -0.09375 to 0.09375
Outputs:
- layer_out: bfloat16 [1536, 8, 6144], P('tok', None, 'wid')
The draws below stay inside these ranges and needn't reach their ends.
All inputs are finite; a program needn't handle non-finite values.
Results may differ from the reference program's by a relative error of at most 0.0034.
The reference program's roundings to bfloat16 on the way (of `normed`, `value`, `probs` and `mixed`) count: a program that leaves them out, or rounds other values in their place, can miss the bound.
Values may be sent and summed in bfloat16 or wider, within the bound.
No kernel may reach another device: no remote copies, remote signals or barrier semaphores. Data moves between devices by JAX's collectives and lax.ppermute only.
A program may use at most 128 MiB of HBM per device.

```python
import jax
import jax.numpy as jnp
from jax import lax

D = 6144
HEADS = 32
HEAD_DIM = 128
PATCHES = 1536
IMAGES = 8
HD = 4096


def base_query(key):
    raw = jnp.clip(jax.random.normal(jax.random.fold_in(key, 11), (D, HD), jnp.float32), -6.0, 6.0)
    return raw * D ** (-0.5)


def draw_w_query(key, part):
    return base_query(key).astype(jnp.bfloat16)


def draw_w_key(key, part):
    noise = jnp.clip(jax.random.normal(jax.random.fold_in(key, 12), (D, HD), jnp.float32), -6.0, 6.0)
    result = noise * D ** (-0.5)
    return result.astype(jnp.bfloat16)


def gain_draw(key, salt):
    result = jax.random.uniform(jax.random.fold_in(key, salt), (HD,), jnp.float32, 0.6, 1.4)
    return result


def draw_q_gain(key, part):
    return gain_draw(key, 21)


def draw_k_gain(key, part):
    return gain_draw(key, 31)


def level_of(key, extent, cuts, low, largest):
    loudness = 1.0
    for position, parts in cuts:
        steps = jax.random.uniform(jax.random.fold_in(jax.random.fold_in(key, 6), position), (parts,), jnp.float32, low / len(cuts), largest / len(cuts))
        loudness = loudness * jnp.repeat(jnp.exp(steps), extent[position] // parts).reshape((-1,) + (1,) * (len(extent) - 1 - position))
    return loudness


def gaussian(rng, extent, deviation, reach, cuts=(), kind=jnp.bfloat16):
    drawn = deviation * jax.random.normal(rng, extent, jnp.float32)
    if cuts:
        drawn = drawn * level_of(rng, extent, cuts, -0.22, 0.18)
    return jnp.clip(drawn, -reach, reach).astype(kind)


def setup_inputs(seed: int = 0) -> dict:
    seeds = jax.random.split(jax.random.key(seed), 8)
    return {
        "patches": gaussian(seeds[0], (PATCHES, IMAGES, D), 1.0, 6.0, ((0, 16), (2, 8))),
        "w_query": draw_w_query(jax.random.fold_in(seeds[7], 71), 0),
        "w_key": draw_w_key(jax.random.fold_in(seeds[7], 71), 0),
        "w_value": gaussian(seeds[3], (D, HD), D ** -0.5, 0.078125, ((0, 16), (1, 8))),
        "q_gain": draw_q_gain(jax.random.fold_in(seeds[7], 71), 0),
        "k_gain": draw_k_gain(jax.random.fold_in(seeds[7], 71), 0),
        "w_out": gaussian(seeds[6], (HD, D), HD ** -0.5, 0.09375, ((0, 16), (1, 8))),
    }


def layer_norm_rows(values, eps):
    mean = lax.optimization_barrier(jnp.mean(values, axis=-1, keepdims=True))
    var = lax.optimization_barrier(jnp.mean(values * values, axis=-1, keepdims=True)) - mean * mean
    return (values - mean) * lax.rsqrt(var + eps)

def reference(patches, w_query, w_key, w_value, q_gain, k_gain, w_out):
    flat = patches.reshape(PATCHES * IMAGES, D).astype(jnp.float32)
    normed = layer_norm_rows(flat, 1e-06).astype(jnp.bfloat16)
    query = jnp.dot(normed, w_query, preferred_element_type=jnp.float32)
    key = jnp.dot(normed, w_key, preferred_element_type=jnp.float32)
    value = jnp.dot(normed, w_value, preferred_element_type=jnp.float32).astype(jnp.bfloat16)
    query = query.reshape(PATCHES, IMAGES, HEADS, HEAD_DIM)
    key = key.reshape(PATCHES, IMAGES, HEADS, HEAD_DIM)
    qnorm = (layer_norm_rows(query, 1e-06) * q_gain.reshape(HEADS, HEAD_DIM)).astype(jnp.bfloat16)
    knorm = (layer_norm_rows(key, 1e-06) * k_gain.reshape(HEADS, HEAD_DIM)).astype(jnp.bfloat16)
    value = value.reshape(PATCHES, IMAGES, HEADS, HEAD_DIM)
    items_q = jnp.transpose(qnorm.reshape(PATCHES, IMAGES * HEADS, HEAD_DIM), (1, 0, 2))
    items_k = jnp.transpose(knorm.reshape(PATCHES, IMAGES * HEADS, HEAD_DIM), (1, 0, 2))
    items_v = jnp.transpose(value.reshape(PATCHES, IMAGES * HEADS, HEAD_DIM), (1, 0, 2))
    scale = HEAD_DIM ** (-0.5)

    def attend(triple):
        qitem, kitem, vitem = triple
        scores = jnp.dot(qitem.astype(jnp.float32), kitem.astype(jnp.float32).T) * scale
        top = lax.optimization_barrier(jnp.max(scores, axis=-1, keepdims=True))
        expo = jnp.exp(scores - top)
        probs = (expo / lax.optimization_barrier(jnp.sum(expo, axis=-1, keepdims=True))).astype(jnp.bfloat16)
        return jnp.dot(probs, vitem, preferred_element_type=jnp.float32).astype(jnp.bfloat16)
    mixed = lax.map(attend, (items_q, items_k, items_v))
    mixed = jnp.transpose(mixed, (1, 0, 2)).reshape(PATCHES * IMAGES, HD)
    branch = jnp.dot(mixed, w_out, preferred_element_type=jnp.float32)
    return (flat + branch).astype(jnp.bfloat16).reshape(PATCHES, IMAGES, D)
```

```python
import jax
import jax.numpy as jnp
from jax import lax
from jax.sharding import PartitionSpec as P

D = 6144
HEAD_DIM = 128
HD = 4096
RING = 4


def layer_norm_rows(values, eps):
    mean = jnp.mean(values, axis=-1, keepdims=True)
    var = jnp.mean(values * values, axis=-1, keepdims=True) - mean * mean
    return (values - mean) * lax.rsqrt(var + eps)


def add_rows(left, piece):
    return jnp.dot(left, piece, preferred_element_type=jnp.float32)


def head_norm(values, gain, eps):
    rows, images, width = values.shape
    heads_here = width // HEAD_DIM
    shaped = values.reshape(rows, images, heads_here, HEAD_DIM)
    normed = layer_norm_rows(shaped, eps) * gain.reshape(heads_here, HEAD_DIM)
    return normed.astype(jnp.bfloat16).reshape(rows, images * heads_here, HEAD_DIM)


def shift_pairs(sx, sy):
    return [
        (x * RING + y, ((x + sx) % RING) * RING + (y + sy) % RING)
        for x in range(RING)
        for y in range(RING)
    ]


def ring_step(group, along_x):
    sx, sy = (1, 0) if along_x else (0, 1)
    from_minus = lax.ppermute(group, "tok", shift_pairs(sx, sy))
    from_plus = lax.ppermute(group, "tok", shift_pairs(-sx, -sy))
    half = group.shape[-1] // 2
    first = lax.ppermute(from_minus[..., :half], "tok", shift_pairs(sx, sy))
    second = lax.ppermute(from_plus[..., half:], "tok", shift_pairs(-sx, -sy))
    across = jnp.concatenate([first, second], axis=-1)
    return [group, from_plus, across, from_minus]


def place(blocks, start, lead):
    out = jnp.zeros((RING,) + blocks[0].shape, blocks[0].dtype)
    for k, block in enumerate(blocks):
        out = lax.dynamic_update_slice(out, block[None], ((start + k) % RING,) + (0,) * block.ndim)
    return out


def ring_gather(block):
    rows, cols = block.shape
    t = lax.axis_index("tok")
    xi, yi = t // RING, t % RING
    half = cols // 2
    parts = []
    for y_first, piece in ((True, block[:, :half]), (False, block[:, half:])):
        inner = place(ring_step(piece, not y_first), yi if y_first else xi, 0)
        outer = place(ring_step(inner, y_first), xi if y_first else yi, 0)
        if not y_first:
            outer = jnp.swapaxes(outer, 0, 1)
        parts.append(outer.reshape(RING * RING * rows, -1))
    return jnp.concatenate(parts, axis=-1)


def local(patches, w_query, w_key, w_value, q_gain, k_gain, w_out):
    local_rows, images, local_width = patches.shape
    whole_raw = lax.all_gather(patches, "wid", axis=2, tiled=True)
    flat = layer_norm_rows(whole_raw.astype(jnp.float32), 1e-06).astype(jnp.bfloat16)
    flat = flat.reshape(local_rows * images, D)

    def add_one(piece):
        return add_rows(flat, piece)

    query = add_one(ring_gather(w_query))
    key = add_one(ring_gather(w_key))
    value = add_one(lax.all_gather(w_value, "tok", axis=0, tiled=True))
    head_width = query.shape[1]
    heads_here = head_width // HEAD_DIM
    qnorm = head_norm(query.reshape(local_rows, images, head_width), q_gain, 1e-06)
    knorm = head_norm(key.reshape(local_rows, images, head_width), k_gain, 1e-06)
    vshaped = value.astype(jnp.bfloat16).reshape(local_rows, images * heads_here, HEAD_DIM)
    qfull, kfull, vfull = (
        lax.all_to_all(qnorm, "tok", split_axis=1, concat_axis=0, tiled=True),
        lax.all_to_all(knorm, "tok", split_axis=1, concat_axis=0, tiled=True),
        lax.all_to_all(vshaped, "tok", split_axis=1, concat_axis=0, tiled=True),
    )
    seq_rows, item_count, _ = qfull.shape
    block = min(512, seq_rows)
    blocks = qfull.reshape(seq_rows // block, block, item_count, HEAD_DIM)
    scale = HEAD_DIM ** (-0.5)

    def attend(qblock):
        scores = (
            jnp.einsum("qid,kid->iqk", qblock, kfull, preferred_element_type=jnp.float32) * scale
        )
        top = jnp.max(scores, axis=-1, keepdims=True)
        expo = jnp.exp(scores - top)
        probs = (expo / jnp.sum(expo, axis=-1, keepdims=True)).astype(jnp.bfloat16)
        return jnp.einsum("iqk,kid->qid", probs, vfull, preferred_element_type=jnp.float32).astype(
            jnp.bfloat16
        )

    attended = lax.map(attend, blocks).reshape(seq_rows, item_count, HEAD_DIM)
    returned = lax.all_to_all(attended, "tok", split_axis=0, concat_axis=1, tiled=True)
    mixed = returned.reshape(local_rows, images, head_width)
    mixed_whole = lax.all_gather(mixed, "wid", axis=2, tiled=True).reshape(local_rows * images, HD)
    branch = add_rows(mixed_whole, ring_gather(w_out))
    as_float = patches.astype(jnp.float32)
    return (as_float + branch.reshape(local_rows, images, local_width)).astype(jnp.bfloat16)


def solution(mesh):
    placed = (
        P("tok", None, "wid"),
        P("tok", "wid"),
        P("tok", "wid"),
        P("tok", "wid"),
        P("wid"),
        P("wid"),
        P("tok", "wid"),
    )
    return jax.shard_map(
        local, mesh=mesh, in_specs=placed, out_specs=P("tok", None, "wid"), check_vma=False
    )
```

```python
import jax
import jax.numpy as jnp
from jax import lax
from jax.sharding import PartitionSpec as P

D = 6144
HEAD_DIM = 128
HD = 4096
RING = 4


def layer_norm_rows(values, eps):
    mean = jnp.mean(values, axis=-1, keepdims=True)
    var = jnp.mean(values * values, axis=-1, keepdims=True) - mean * mean
    return (values - mean) * lax.rsqrt(var + eps)


def add_rows(left, piece):
    return jnp.dot(left, piece, preferred_element_type=jnp.float32)


def head_norm(values, gain, eps):
    rows, images, width = values.shape
    heads_here = width // HEAD_DIM
    shaped = values.reshape(rows, images, heads_here, HEAD_DIM)
    normed = layer_norm_rows(shaped, eps) * gain.reshape(heads_here, HEAD_DIM)
    return normed.astype(jnp.bfloat16).reshape(rows, images * heads_here, HEAD_DIM)


def shift_pairs(sx, sy):
    return [
        (x * RING + y, ((x + sx) % RING) * RING + (y + sy) % RING)
        for x in range(RING)
        for y in range(RING)
    ]


def ring_step(group, along_x):
    sx, sy = (1, 0) if along_x else (0, 1)
    from_minus = lax.ppermute(group, "tok", shift_pairs(sx, sy))
    from_plus = lax.ppermute(group, "tok", shift_pairs(-sx, -sy))
    half = group.shape[-1] // 2
    first = lax.ppermute(from_minus[..., :half], "tok", shift_pairs(sx, sy))
    second = lax.ppermute(from_plus[..., half:], "tok", shift_pairs(-sx, -sy))
    across = jnp.concatenate([first, second], axis=-1)
    return [group, from_plus, across, from_minus]


def ring_gather(blocks):
    half = blocks.shape[-1] // 2
    parts = []
    for y_first, piece in ((True, blocks[..., :half]), (False, blocks[..., half:])):
        inner = jnp.stack(ring_step(piece, not y_first), axis=1)
        outer = jnp.stack(ring_step(inner, y_first), axis=1)
        if not y_first:
            outer = jnp.swapaxes(outer, 1, 2)
        parts.append(outer)
    whole = jnp.concatenate(parts, axis=-1)
    m, rows, cols = blocks.shape
    return whole.reshape(m, RING * RING * rows, cols)


def roll_blocks(values):
    t = lax.axis_index("tok")
    out = values
    for axis, shift in ((-3, t // RING), (-2, t % RING)):
        doubled = jnp.concatenate([out, out], axis=axis)
        starts = [0] * out.ndim
        starts[out.ndim + axis] = shift
        out = lax.dynamic_slice(doubled, starts, out.shape)
    return out


def local(patches, w_query, w_key, w_value, q_gain, k_gain, w_out):
    local_rows, images, local_width = patches.shape
    whole_raw = lax.all_gather(patches, "wid", axis=2, tiled=True)
    rolled = roll_blocks(whole_raw.reshape(local_rows, images, RING, RING, D // (RING * RING)))
    rolled = rolled.reshape(local_rows * images, D)
    flat = layer_norm_rows(rolled.astype(jnp.float32), 1e-06).astype(jnp.bfloat16)

    gathered = ring_gather(jnp.stack([w_query, w_key, w_value]))
    query = add_rows(flat, gathered[0])
    key = add_rows(flat, gathered[1])
    value = add_rows(flat, gathered[2])
    head_width = query.shape[1]
    heads_here = head_width // HEAD_DIM
    qnorm = head_norm(query.reshape(local_rows, images, head_width), q_gain, 1e-06)
    knorm = head_norm(key.reshape(local_rows, images, head_width), k_gain, 1e-06)
    vshaped = value.astype(jnp.bfloat16).reshape(local_rows, images * heads_here, HEAD_DIM)
    qfull, kfull, vfull = (
        lax.all_to_all(qnorm, "tok", split_axis=1, concat_axis=0, tiled=True),
        lax.all_to_all(knorm, "tok", split_axis=1, concat_axis=0, tiled=True),
        lax.all_to_all(vshaped, "tok", split_axis=1, concat_axis=0, tiled=True),
    )
    seq_rows, item_count, _ = qfull.shape
    block = min(512, seq_rows)
    blocks = qfull.reshape(seq_rows // block, block, item_count, HEAD_DIM)
    scale = HEAD_DIM ** (-0.5)

    def attend(qblock):
        scores = (
            jnp.einsum("qid,kid->iqk", qblock, kfull, preferred_element_type=jnp.float32) * scale
        )
        top = jnp.max(scores, axis=-1, keepdims=True)
        expo = jnp.exp(scores - top)
        probs = (expo / jnp.sum(expo, axis=-1, keepdims=True)).astype(jnp.bfloat16)
        return jnp.einsum("iqk,kid->qid", probs, vfull, preferred_element_type=jnp.float32).astype(
            jnp.bfloat16
        )

    attended = lax.map(attend, blocks).reshape(seq_rows, item_count, HEAD_DIM)
    returned = lax.all_to_all(attended, "tok", split_axis=0, concat_axis=1, tiled=True)
    mixed = returned.reshape(local_rows, images, head_width)
    mixed_whole = lax.all_gather(mixed, "wid", axis=2, tiled=True).reshape(local_rows * images, HD)
    branch = add_rows(mixed_whole, lax.all_gather(w_out, "tok", axis=0, tiled=True))
    as_float = patches.astype(jnp.float32)
    return (as_float + branch.reshape(local_rows, images, local_width)).astype(jnp.bfloat16)


def solution(mesh):
    placed = (
        P("tok", None, "wid"),
        P("tok", "wid"),
        P("tok", "wid"),
        P("tok", "wid"),
        P("wid"),
        P("wid"),
        P("tok", "wid"),
    )
    return jax.shard_map(
        local, mesh=mesh, in_specs=placed, out_specs=P("tok", None, "wid"), check_vma=False
    )
```

```python
import jax
import jax.numpy as jnp
from jax import lax
from jax.sharding import PartitionSpec as P

D = 6144
HEAD_DIM = 128
HD = 4096
RING = 4


def layer_norm_rows(values, eps):
    mean = jnp.mean(values, axis=-1, keepdims=True)
    var = jnp.mean(values * values, axis=-1, keepdims=True) - mean * mean
    return (values - mean) * lax.rsqrt(var + eps)


def add_rows(left, piece):
    return jnp.dot(left, piece, preferred_element_type=jnp.float32)


def head_norm(values, gain, eps):
    rows, images, width = values.shape
    heads_here = width // HEAD_DIM
    shaped = values.reshape(rows, images, heads_here, HEAD_DIM)
    normed = layer_norm_rows(shaped, eps) * gain.reshape(heads_here, HEAD_DIM)
    return normed.astype(jnp.bfloat16).reshape(rows, images * heads_here, HEAD_DIM)


def shift_pairs(sx, sy):
    return [
        (x * RING + y, ((x + sx) % RING) * RING + (y + sy) % RING)
        for x in range(RING)
        for y in range(RING)
    ]


def ring_step(group, along_x):
    sx, sy = (1, 0) if along_x else (0, 1)
    from_minus = lax.ppermute(group, "tok", shift_pairs(sx, sy))
    from_plus = lax.ppermute(group, "tok", shift_pairs(-sx, -sy))
    half = group.shape[-1] // 2
    first = lax.ppermute(from_minus[..., :half], "tok", shift_pairs(sx, sy))
    second = lax.ppermute(from_plus[..., half:], "tok", shift_pairs(-sx, -sy))
    across = jnp.concatenate([first, second], axis=-1)
    return [group, from_plus, across, from_minus]


def ring_gather(blocks):
    half = blocks.shape[-1] // 2
    parts = []
    for y_first, piece in ((True, blocks[..., :half]), (False, blocks[..., half:])):
        inner = jnp.stack(ring_step(piece, not y_first), axis=1)
        outer = jnp.stack(ring_step(inner, y_first), axis=1)
        if not y_first:
            outer = jnp.swapaxes(outer, 1, 2)
        parts.append(outer)
    whole = jnp.concatenate(parts, axis=-1)
    m, rows, cols = blocks.shape
    return whole.reshape(m, RING * RING * rows, cols)


def roll_major(values):
    t = lax.axis_index("tok")
    out = values
    for axis, shift in ((0, t // RING), (1, t % RING)):
        doubled = jnp.concatenate([out, out], axis=axis)
        starts = [0] * out.ndim
        starts[axis] = shift
        out = lax.dynamic_slice(doubled, starts, out.shape)
    return out


def contract_blocks(blocks, weight):
    rows = blocks.shape[-1]
    shaped = weight.reshape(RING, RING, rows, weight.shape[-1])
    return jnp.einsum("abtr,abrc->tc", blocks, shaped, preferred_element_type=jnp.float32)


def local(patches, w_query, w_key, w_value, q_gain, k_gain, w_out):
    local_rows, images, local_width = patches.shape
    tokens = local_rows * images
    sub = D // (RING * RING)
    pieces = patches.reshape(tokens, local_width // sub, sub).transpose(1, 0, 2)
    whole_raw = lax.all_gather(pieces, "wid", axis=0, tiled=True).astype(jnp.float32)
    mean = jnp.mean(whole_raw, axis=(0, 2), keepdims=True)
    var = jnp.mean(whole_raw * whole_raw, axis=(0, 2), keepdims=True) - mean * mean
    normed = ((whole_raw - mean) * lax.rsqrt(var + 1e-06)).astype(jnp.bfloat16)
    normed = normed.reshape(RING, RING, tokens, sub)
    rolled = roll_major(normed)

    gathered = ring_gather(jnp.stack([w_query, w_key]))
    query = contract_blocks(rolled, gathered[0])
    key = contract_blocks(rolled, gathered[1])
    value = contract_blocks(normed, lax.all_gather(w_value, "tok", axis=0, tiled=True))
    head_width = query.shape[1]
    heads_here = head_width // HEAD_DIM
    qnorm = head_norm(query.reshape(local_rows, images, head_width), q_gain, 1e-06)
    knorm = head_norm(key.reshape(local_rows, images, head_width), k_gain, 1e-06)
    vshaped = value.astype(jnp.bfloat16).reshape(local_rows, images * heads_here, HEAD_DIM)
    qfull, kfull, vfull = (
        lax.all_to_all(qnorm, "tok", split_axis=1, concat_axis=0, tiled=True),
        lax.all_to_all(knorm, "tok", split_axis=1, concat_axis=0, tiled=True),
        lax.all_to_all(vshaped, "tok", split_axis=1, concat_axis=0, tiled=True),
    )
    seq_rows, item_count, _ = qfull.shape
    block = min(512, seq_rows)
    blocks = qfull.reshape(seq_rows // block, block, item_count, HEAD_DIM)
    scale = HEAD_DIM ** (-0.5)

    def attend(qblock):
        scores = (
            jnp.einsum("qid,kid->iqk", qblock, kfull, preferred_element_type=jnp.float32) * scale
        )
        top = jnp.max(scores, axis=-1, keepdims=True)
        expo = jnp.exp(scores - top)
        probs = (expo / jnp.sum(expo, axis=-1, keepdims=True)).astype(jnp.bfloat16)
        return jnp.einsum("iqk,kid->qid", probs, vfull, preferred_element_type=jnp.float32).astype(
            jnp.bfloat16
        )

    attended = lax.map(attend, blocks).reshape(seq_rows, item_count, HEAD_DIM)
    returned = lax.all_to_all(attended, "tok", split_axis=0, concat_axis=1, tiled=True)
    mixed = returned.reshape(local_rows, images, head_width)
    mixed_whole = lax.all_gather(mixed, "wid", axis=2, tiled=True).reshape(tokens, HD)
    branch = add_rows(mixed_whole, lax.all_gather(w_out, "tok", axis=0, tiled=True))
    as_float = patches.astype(jnp.float32)
    return (as_float + branch.reshape(local_rows, images, local_width)).astype(jnp.bfloat16)


def solution(mesh):
    placed = (
        P("tok", None, "wid"),
        P("tok", "wid"),
        P("tok", "wid"),
        P("tok", "wid"),
        P("wid"),
        P("wid"),
        P("tok", "wid"),
    )
    return jax.shard_map(
        local, mesh=mesh, in_specs=placed, out_specs=P("tok", None, "wid"), check_vma=False
    )
```

```python
import jax
import jax.numpy as jnp
from jax import lax
from jax.sharding import PartitionSpec as P


D = 6144
HEAD_DIM = 128
HD = 4096
RING = 4


def layer_norm_rows(values, eps):
    mean = jnp.mean(values, axis=-1, keepdims=True)
    var = jnp.mean(values * values, axis=-1, keepdims=True) - mean * mean
    return (values - mean) * lax.rsqrt(var + eps)


def add_rows(left, piece):
    return jnp.dot(left, piece, preferred_element_type=jnp.float32)


def head_norm(values, gain, eps):
    rows, images, width = values.shape
    heads_here = width // HEAD_DIM
    shaped = values.reshape(rows, images, heads_here, HEAD_DIM)
    normed = layer_norm_rows(shaped, eps) * gain.reshape(heads_here, HEAD_DIM)
    return normed.astype(jnp.bfloat16).reshape(rows, images * heads_here, HEAD_DIM)


def shift_pairs(sx, sy):
    return [
        (x * RING + y, ((x + sx) % RING) * RING + (y + sy) % RING)
        for x in range(RING)
        for y in range(RING)
    ]


def ring_step(group, along_x):
    sx, sy = (1, 0) if along_x else (0, 1)
    from_minus = lax.ppermute(group, "tok", shift_pairs(sx, sy))
    from_plus = lax.ppermute(group, "tok", shift_pairs(-sx, -sy))
    half = group.shape[-1] // 2
    first = lax.ppermute(from_minus[..., :half], "tok", shift_pairs(sx, sy))
    second = lax.ppermute(from_plus[..., half:], "tok", shift_pairs(-sx, -sy))
    across = jnp.concatenate([first, second], axis=-1)
    return [group, from_plus, across, from_minus]


def ring_gather(blocks):
    half = blocks.shape[-1] // 2
    parts = []
    for y_first, piece in ((True, blocks[..., :half]), (False, blocks[..., half:])):
        inner = jnp.stack(ring_step(piece, not y_first), axis=1)
        outer = jnp.stack(ring_step(inner, y_first), axis=1)
        if not y_first:
            outer = jnp.swapaxes(outer, 1, 2)
        parts.append(outer)
    whole = jnp.concatenate(parts, axis=-1)
    m, rows, cols = blocks.shape
    return whole.reshape(m, RING * RING * rows, cols)


def roll_major(values):
    t = lax.axis_index("tok")
    out = values
    for axis, shift in ((0, t // RING), (1, t % RING)):
        doubled = jnp.concatenate([out, out], axis=axis)
        starts = [0] * out.ndim
        starts[axis] = shift
        out = lax.dynamic_slice(doubled, starts, out.shape)
    return out


def contract_blocks(blocks, weight):
    rows = blocks.shape[-1]
    shaped = weight.reshape(RING, RING, rows, weight.shape[-1])
    return jnp.einsum("abtr,abrc->tc", blocks, shaped, preferred_element_type=jnp.float32)


def local(patches, w_query, w_key, w_value, q_gain, k_gain, w_out):
    local_rows, images, local_width = patches.shape
    tokens = local_rows * images
    sub = D // (RING * RING)
    pieces = patches.reshape(tokens, local_width // sub, sub).transpose(1, 0, 2)
    whole_raw = lax.all_gather(pieces, "wid", axis=0, tiled=True).astype(jnp.float32)
    mean = jnp.mean(whole_raw, axis=(0, 2), keepdims=True)
    var = jnp.mean(whole_raw * whole_raw, axis=(0, 2), keepdims=True) - mean * mean
    normed = ((whole_raw - mean) * lax.rsqrt(var + 1e-06)).astype(jnp.bfloat16)
    normed = normed.reshape(RING, RING, tokens, sub)
    rolled = roll_major(normed)

    gathered = ring_gather(jnp.stack([w_query, w_key]))
    query = contract_blocks(rolled, gathered[0])
    key = contract_blocks(rolled, gathered[1])
    value = contract_blocks(normed, lax.all_gather(w_value, "tok", axis=0, tiled=True))
    head_width = query.shape[1]
    heads_here = head_width // HEAD_DIM
    qnorm = head_norm(query.reshape(local_rows, images, head_width), q_gain, 1e-06)
    knorm = head_norm(key.reshape(local_rows, images, head_width), k_gain, 1e-06)
    vshaped = value.astype(jnp.bfloat16).reshape(local_rows, images * heads_here, HEAD_DIM)
    stacked = jnp.stack([qnorm, knorm, vshaped], axis=1)
    spread = lax.all_to_all(stacked, "tok", split_axis=2, concat_axis=0, tiled=True)
    qfull, kfull, vfull = spread[:, 0], spread[:, 1], spread[:, 2]
    seq_rows, item_count, _ = qfull.shape
    block = seq_rows
    blocks = qfull.reshape(seq_rows // block, block, item_count, HEAD_DIM)
    scale = HEAD_DIM ** (-0.5)

    def attend(qblock):
        scores = (
            jnp.einsum("qid,kid->iqk", qblock, kfull, preferred_element_type=jnp.float32) * scale
        )
        top = jnp.max(scores, axis=-1, keepdims=True)
        expo = jnp.exp(scores - top)
        probs = (expo / jnp.sum(expo, axis=-1, keepdims=True)).astype(jnp.bfloat16)
        return jnp.einsum("iqk,kid->qid", probs, vfull, preferred_element_type=jnp.float32).astype(
            jnp.bfloat16
        )

    attended = lax.map(attend, blocks).reshape(seq_rows, item_count, HEAD_DIM)
    returned = lax.all_to_all(attended, "tok", split_axis=0, concat_axis=1, tiled=True)
    mixed = returned.reshape(local_rows, images, head_width)
    mixed_whole = lax.all_gather(mixed, "wid", axis=2, tiled=True).reshape(tokens, HD)
    branch = add_rows(mixed_whole, lax.all_gather(w_out, "tok", axis=0, tiled=True))
    as_float = patches.astype(jnp.float32)
    return (as_float + branch.reshape(local_rows, images, local_width)).astype(jnp.bfloat16)


def solution(mesh):
    placed = (
        P("tok", None, "wid"),
        P("tok", "wid"),
        P("tok", "wid"),
        P("tok", "wid"),
        P("wid"),
        P("wid"),
        P("tok", "wid"),
    )

    return jax.shard_map(
        local, mesh=mesh, in_specs=placed, out_specs=P("tok", None, "wid"), check_vma=False
    )
```

```python
import jax
import jax.numpy as jnp
from jax import lax
from jax.sharding import PartitionSpec as P


D = 6144
HEAD_DIM = 128
HD = 4096
RING = 4


def layer_norm_rows(values, eps):
    mean = jnp.mean(values, axis=-1, keepdims=True)
    var = jnp.mean(values * values, axis=-1, keepdims=True) - mean * mean
    return (values - mean) * lax.rsqrt(var + eps)


def add_rows(left, piece):
    return jnp.dot(left, piece, preferred_element_type=jnp.float32)


def head_norm(values, gain, eps):
    rows, images, width = values.shape
    heads_here = width // HEAD_DIM
    shaped = values.reshape(rows, images, heads_here, HEAD_DIM)
    normed = layer_norm_rows(shaped, eps) * gain.reshape(heads_here, HEAD_DIM)
    return normed.astype(jnp.bfloat16).reshape(rows, images * heads_here, HEAD_DIM)


def shift_pairs(sx, sy):
    return [
        (x * RING + y, ((x + sx) % RING) * RING + (y + sy) % RING)
        for x in range(RING)
        for y in range(RING)
    ]


def ring_step(group, along_x):
    sx, sy = (1, 0) if along_x else (0, 1)
    from_minus = lax.ppermute(group, "tok", shift_pairs(sx, sy))
    from_plus = lax.ppermute(group, "tok", shift_pairs(-sx, -sy))
    half = group.shape[-1] // 2
    first = lax.ppermute(from_minus[..., :half], "tok", shift_pairs(sx, sy))
    second = lax.ppermute(from_plus[..., half:], "tok", shift_pairs(-sx, -sy))
    across = jnp.concatenate([first, second], axis=-1)
    return [group, from_plus, across, from_minus]


def ring_project(rolled, blocks):
    half = blocks.shape[-1] // 2
    parts = []
    for y_first, piece in ((True, blocks[..., :half]), (False, blocks[..., half:])):
        inner = jnp.stack(ring_step(piece, not y_first), axis=1)
        outer = ring_step(inner, y_first)
        total = None
        for k, got in enumerate(outer):
            lhs = rolled[k] if y_first else rolled[:, k]
            term = jnp.einsum("btr,mbrc->mtc", lhs, got, preferred_element_type=jnp.float32)
            total = term if total is None else total + term
        parts.append(total)
    return jnp.concatenate(parts, axis=-1)


def roll_major(values):
    t = lax.axis_index("tok")
    out = values
    for axis, shift in ((0, t // RING), (1, t % RING)):
        doubled = jnp.concatenate([out, out], axis=axis)
        starts = [0] * out.ndim
        starts[axis] = shift
        out = lax.dynamic_slice(doubled, starts, out.shape)
    return out


def contract_blocks(blocks, weight):
    rows = blocks.shape[-1]
    shaped = weight.reshape(RING, RING, rows, weight.shape[-1])
    return jnp.einsum("abtr,abrc->tc", blocks, shaped, preferred_element_type=jnp.float32)


def local(patches, w_query, w_key, w_value, q_gain, k_gain, w_out):
    local_rows, images, local_width = patches.shape
    tokens = local_rows * images
    sub = D // (RING * RING)
    pieces = patches.reshape(tokens, local_width // sub, sub).transpose(1, 0, 2)
    whole_raw = lax.all_gather(pieces, "wid", axis=0, tiled=True).astype(jnp.float32)
    mean = jnp.mean(whole_raw, axis=(0, 2), keepdims=True)
    var = jnp.mean(whole_raw * whole_raw, axis=(0, 2), keepdims=True) - mean * mean
    normed = ((whole_raw - mean) * lax.rsqrt(var + 1e-06)).astype(jnp.bfloat16)
    normed = normed.reshape(RING, RING, tokens, sub)
    rolled = roll_major(normed)

    projected = ring_project(rolled, jnp.stack([w_query, w_key]))
    query = projected[0]
    key = projected[1]
    value = contract_blocks(normed, lax.all_gather(w_value, "tok", axis=0, tiled=True))
    head_width = query.shape[1]
    heads_here = head_width // HEAD_DIM
    qnorm = head_norm(query.reshape(local_rows, images, head_width), q_gain, 1e-06)
    knorm = head_norm(key.reshape(local_rows, images, head_width), k_gain, 1e-06)
    vshaped = value.astype(jnp.bfloat16).reshape(local_rows, images * heads_here, HEAD_DIM)
    stacked = jnp.stack([qnorm, knorm, vshaped], axis=1)
    spread = lax.all_to_all(stacked, "tok", split_axis=2, concat_axis=0, tiled=True)
    qfull, kfull, vfull = spread[:, 0], spread[:, 1], spread[:, 2]
    seq_rows, item_count, _ = qfull.shape
    block = seq_rows
    blocks = qfull.reshape(seq_rows // block, block, item_count, HEAD_DIM)
    scale = HEAD_DIM ** (-0.5)

    def attend(qblock):
        scores = (
            jnp.einsum("qid,kid->iqk", qblock, kfull, preferred_element_type=jnp.float32) * scale
        )
        top = jnp.max(scores, axis=-1, keepdims=True)
        expo = jnp.exp(scores - top)
        probs = (expo / jnp.sum(expo, axis=-1, keepdims=True)).astype(jnp.bfloat16)
        return jnp.einsum("iqk,kid->qid", probs, vfull, preferred_element_type=jnp.float32).astype(
            jnp.bfloat16
        )

    attended = lax.map(attend, blocks).reshape(seq_rows, item_count, HEAD_DIM)
    returned = lax.all_to_all(attended, "tok", split_axis=0, concat_axis=1, tiled=True)
    mixed = returned.reshape(local_rows, images, head_width)
    mixed_whole = lax.all_gather(mixed, "wid", axis=2, tiled=True).reshape(tokens, HD)
    branch = add_rows(mixed_whole, lax.all_gather(w_out, "tok", axis=0, tiled=True))
    as_float = patches.astype(jnp.float32)
    return (as_float + branch.reshape(local_rows, images, local_width)).astype(jnp.bfloat16)


def solution(mesh):
    placed = (
        P("tok", None, "wid"),
        P("tok", "wid"),
        P("tok", "wid"),
        P("tok", "wid"),
        P("wid"),
        P("wid"),
        P("tok", "wid"),
    )

    return jax.shard_map(
        local, mesh=mesh, in_specs=placed, out_specs=P("tok", None, "wid"), check_vma=False
    )
```

```python
import jax
import jax.numpy as jnp
from jax import lax
from jax.sharding import PartitionSpec as P


D = 6144
HEAD_DIM = 128
HD = 4096
RING = 4


def layer_norm_rows(values, eps):
    mean = jnp.mean(values, axis=-1, keepdims=True)
    var = jnp.mean(values * values, axis=-1, keepdims=True) - mean * mean
    return (values - mean) * lax.rsqrt(var + eps)


def add_rows(left, piece):
    return jnp.dot(left, piece, preferred_element_type=jnp.float32)


def head_norm(values, gain, eps):
    rows, images, width = values.shape
    heads_here = width // HEAD_DIM
    shaped = values.reshape(rows, images, heads_here, HEAD_DIM)
    normed = layer_norm_rows(shaped, eps) * gain.reshape(heads_here, HEAD_DIM)
    return normed.astype(jnp.bfloat16).reshape(rows, images * heads_here, HEAD_DIM)


def shift_pairs(sx, sy):
    return [
        (x * RING + y, ((x + sx) % RING) * RING + (y + sy) % RING)
        for x in range(RING)
        for y in range(RING)
    ]


def ring_step(group, along_x):
    sx, sy = (1, 0) if along_x else (0, 1)
    from_minus = lax.ppermute(group, "tok", shift_pairs(sx, sy))
    from_plus = lax.ppermute(group, "tok", shift_pairs(-sx, -sy))
    half = group.shape[-1] // 2
    first = lax.ppermute(from_minus[..., :half], "tok", shift_pairs(sx, sy))
    second = lax.ppermute(from_plus[..., half:], "tok", shift_pairs(-sx, -sy))
    across = jnp.concatenate([first, second], axis=-1)
    return [group, from_plus, across, from_minus]


def ring_project(rolled, blocks):
    half = blocks.shape[-1] // 2
    parts = []
    for y_first, piece in ((True, blocks[..., :half]), (False, blocks[..., half:])):
        inner = jnp.stack(ring_step(piece, not y_first), axis=1)
        outer = ring_step(inner, y_first)
        total = None
        for k, got in enumerate(outer):
            lhs = rolled[k] if y_first else rolled[:, k]
            term = jnp.einsum("btr,mbrc->mtc", lhs, got, preferred_element_type=jnp.float32)
            total = term if total is None else total + term
        parts.append(total)
    return jnp.concatenate(parts, axis=-1)


def roll_major(values):
    t = lax.axis_index("tok")
    out = values
    for axis, shift in ((0, t // RING), (1, t % RING)):
        doubled = jnp.concatenate([out, out], axis=axis)
        starts = [0] * out.ndim
        starts[axis] = shift
        out = lax.dynamic_slice(doubled, starts, out.shape)
    return out


def contract_blocks(blocks, weight):
    rows = blocks.shape[-1]
    shaped = weight.reshape(RING, RING, rows, weight.shape[-1])
    return jnp.einsum("abtr,abrc->tc", blocks, shaped, preferred_element_type=jnp.float32)


def local(patches, w_query, w_key, w_value, q_gain, k_gain, w_out):
    local_rows, images, local_width = patches.shape
    tokens = local_rows * images
    sub = D // (RING * RING)
    pieces = patches.reshape(tokens, local_width // sub, sub).transpose(1, 0, 2)
    whole_raw = lax.all_gather(pieces, "wid", axis=0, tiled=True).astype(jnp.float32)
    mean = jnp.mean(whole_raw, axis=(0, 2), keepdims=True)
    var = jnp.mean(whole_raw * whole_raw, axis=(0, 2), keepdims=True) - mean * mean
    normed = ((whole_raw - mean) * lax.rsqrt(var + 1e-06)).astype(jnp.bfloat16)
    normed = normed.reshape(RING, RING, tokens, sub)
    rolled = roll_major(normed)

    projected = ring_project(rolled, jnp.stack([w_query, w_key]))
    query = projected[0]
    key = projected[1]
    value = contract_blocks(normed, lax.all_gather(w_value, "tok", axis=0, tiled=True))
    head_width = query.shape[1]
    heads_here = head_width // HEAD_DIM
    qnorm = head_norm(query.reshape(local_rows, images, head_width), q_gain, 1e-06)
    knorm = head_norm(key.reshape(local_rows, images, head_width), k_gain, 1e-06)
    vshaped = value.astype(jnp.bfloat16).reshape(local_rows, images * heads_here, HEAD_DIM)
    vfull = lax.all_to_all(vshaped, "tok", split_axis=1, concat_axis=0, tiled=True)
    stacked = jnp.stack([qnorm, knorm], axis=1)
    spread = lax.all_to_all(stacked, "tok", split_axis=2, concat_axis=0, tiled=True)
    qfull, kfull = spread[:, 0], spread[:, 1]
    seq_rows, item_count, _ = qfull.shape
    block = seq_rows
    blocks = qfull.reshape(seq_rows // block, block, item_count, HEAD_DIM)
    scale = HEAD_DIM ** (-0.5)

    def attend(qblock):
        scores = (
            jnp.einsum("qid,kid->iqk", qblock, kfull, preferred_element_type=jnp.float32) * scale
        )
        top = jnp.max(scores, axis=-1, keepdims=True)
        expo = jnp.exp(scores - top)
        probs = (expo / jnp.sum(expo, axis=-1, keepdims=True)).astype(jnp.bfloat16)
        return jnp.einsum("iqk,kid->qid", probs, vfull, preferred_element_type=jnp.float32).astype(
            jnp.bfloat16
        )

    attended = lax.map(attend, blocks).reshape(seq_rows, item_count, HEAD_DIM)
    returned = lax.all_to_all(attended, "tok", split_axis=0, concat_axis=1, tiled=True)
    mixed = returned.reshape(local_rows, images, head_width)
    mixed_whole = lax.all_gather(mixed, "wid", axis=2, tiled=True).reshape(tokens, HD)
    branch = add_rows(mixed_whole, lax.all_gather(w_out, "tok", axis=0, tiled=True))
    as_float = patches.astype(jnp.float32)
    return (as_float + branch.reshape(local_rows, images, local_width)).astype(jnp.bfloat16)


def solution(mesh):
    placed = (
        P("tok", None, "wid"),
        P("tok", "wid"),
        P("tok", "wid"),
        P("tok", "wid"),
        P("wid"),
        P("wid"),
        P("tok", "wid"),
    )

    return jax.shard_map(
        local, mesh=mesh, in_specs=placed, out_specs=P("tok", None, "wid"), check_vma=False
    )
```

```python
import jax
import jax.numpy as jnp
from jax import lax
from jax.sharding import PartitionSpec as P


D = 6144
HEAD_DIM = 128
HD = 4096
RING = 4


def layer_norm_rows(values, eps):
    mean = jnp.mean(values, axis=-1, keepdims=True)
    var = jnp.mean(values * values, axis=-1, keepdims=True) - mean * mean
    return (values - mean) * lax.rsqrt(var + eps)


def add_rows(left, piece):
    return jnp.dot(left, piece, preferred_element_type=jnp.float32)


def head_norm(values, gain, eps):
    rows, images, width = values.shape
    heads_here = width // HEAD_DIM
    shaped = values.reshape(rows, images, heads_here, HEAD_DIM)
    normed = layer_norm_rows(shaped, eps) * gain.reshape(heads_here, HEAD_DIM)
    return normed.astype(jnp.bfloat16).reshape(rows, images * heads_here, HEAD_DIM)


def shift_pairs(sx, sy):
    return [
        (x * RING + y, ((x + sx) % RING) * RING + (y + sy) % RING)
        for x in range(RING)
        for y in range(RING)
    ]


def near_pair(group, along_x):
    sx, sy = (1, 0) if along_x else (0, 1)
    from_minus = lax.ppermute(group, "tok", shift_pairs(sx, sy))
    from_plus = lax.ppermute(group, "tok", shift_pairs(-sx, -sy))
    return from_minus, from_plus


def far_block(from_minus, from_plus, along_x):
    sx, sy = (1, 0) if along_x else (0, 1)
    half = from_minus.shape[-1] // 2
    first = lax.ppermute(from_minus[..., :half], "tok", shift_pairs(sx, sy))
    second = lax.ppermute(from_plus[..., half:], "tok", shift_pairs(-sx, -sy))
    return jnp.concatenate([first, second], axis=-1)


def ring_project(rolled, blocks):
    half = blocks.shape[-1] // 2
    pieces = (blocks[..., :half], blocks[..., half:])
    inner_x = (False, True)
    near, far = [], []
    for h in (0, 1):
        near.append(near_pair(pieces[h], inner_x[h]))
    for h in (0, 1):
        far.append(far_block(*near[h], inner_x[h]))
    inner = [
        jnp.stack([pieces[h], near[h][1], far[h], near[h][0]], axis=1) for h in range(2)
    ]
    outer_near = []
    for h in (0, 1):
        outer_near.append(near_pair(inner[h], not inner_x[h]))
    outer_far = [far_block(*outer_near[h], not inner_x[h]) for h in range(2)]
    parts = []
    for h in range(2):
        got_all = [inner[h], outer_near[h][1], outer_far[h], outer_near[h][0]]
        total = None
        for k, got in enumerate(got_all):
            lhs = rolled[k] if h == 0 else rolled[:, k]
            term = jnp.einsum("btr,mbrc->mtc", lhs, got, preferred_element_type=jnp.float32)
            total = term if total is None else total + term
        parts.append(total)
    return jnp.concatenate(parts, axis=-1)


def roll_major(values):
    t = lax.axis_index("tok")
    out = values
    for axis, shift in ((0, t // RING), (1, t % RING)):
        doubled = jnp.concatenate([out, out], axis=axis)
        starts = [0] * out.ndim
        starts[axis] = shift
        out = lax.dynamic_slice(doubled, starts, out.shape)
    return out


def local(patches, w_query, w_key, w_value, q_gain, k_gain, w_out):
    local_rows, images, local_width = patches.shape
    tokens = local_rows * images
    sub = D // (RING * RING)
    pieces = patches.reshape(tokens, local_width // sub, sub).transpose(1, 0, 2)
    whole_raw = lax.all_gather(pieces, "wid", axis=0, tiled=True).astype(jnp.float32)
    mean = jnp.mean(whole_raw, axis=(0, 2), keepdims=True)
    var = jnp.mean(whole_raw * whole_raw, axis=(0, 2), keepdims=True) - mean * mean
    normed = ((whole_raw - mean) * lax.rsqrt(var + 1e-06)).astype(jnp.bfloat16)
    normed = normed.reshape(RING, RING, tokens, sub)
    rolled = roll_major(normed)

    projected = ring_project(rolled, jnp.stack([w_query, w_key, w_value]))
    query = projected[0]
    key = projected[1]
    value = projected[2]
    head_width = query.shape[1]
    heads_here = head_width // HEAD_DIM
    qnorm = head_norm(query.reshape(local_rows, images, head_width), q_gain, 1e-06)
    knorm = head_norm(key.reshape(local_rows, images, head_width), k_gain, 1e-06)
    vshaped = value.astype(jnp.bfloat16).reshape(local_rows, images * heads_here, HEAD_DIM)
    vfull = lax.all_to_all(vshaped, "tok", split_axis=1, concat_axis=0, tiled=True)
    stacked = jnp.stack([qnorm, knorm], axis=1)
    spread = lax.all_to_all(stacked, "tok", split_axis=2, concat_axis=0, tiled=True)
    qfull, kfull = spread[:, 0], spread[:, 1]
    seq_rows, item_count, _ = qfull.shape
    block = seq_rows
    blocks = qfull.reshape(seq_rows // block, block, item_count, HEAD_DIM)
    scale = HEAD_DIM ** (-0.5)

    def attend(qblock):
        scores = (
            jnp.einsum("qid,kid->iqk", qblock, kfull, preferred_element_type=jnp.float32) * scale
        )
        top = jnp.max(scores, axis=-1, keepdims=True)
        expo = jnp.exp(scores - top)
        probs = (expo / jnp.sum(expo, axis=-1, keepdims=True)).astype(jnp.bfloat16)
        return jnp.einsum("iqk,kid->qid", probs, vfull, preferred_element_type=jnp.float32).astype(
            jnp.bfloat16
        )

    attended = lax.map(attend, blocks).reshape(seq_rows, item_count, HEAD_DIM)
    returned = lax.all_to_all(attended, "tok", split_axis=0, concat_axis=1, tiled=True)
    mixed = returned.reshape(local_rows, images, head_width)
    mixed_whole = lax.all_gather(mixed, "wid", axis=2, tiled=True).reshape(tokens, HD)
    branch = add_rows(mixed_whole, lax.all_gather(w_out, "tok", axis=0, tiled=True))
    as_float = patches.astype(jnp.float32)
    return (as_float + branch.reshape(local_rows, images, local_width)).astype(jnp.bfloat16)


def solution(mesh):
    placed = (
        P("tok", None, "wid"),
        P("tok", "wid"),
        P("tok", "wid"),
        P("tok", "wid"),
        P("wid"),
        P("wid"),
        P("tok", "wid"),
    )

    return jax.shard_map(
        local, mesh=mesh, in_specs=placed, out_specs=P("tok", None, "wid"), check_vma=False
    )
```

```python
import jax
import jax.numpy as jnp
from jax import lax
from jax.sharding import PartitionSpec as P


D = 6144
HEAD_DIM = 128
HD = 4096
RING = 4


def layer_norm_rows(values, eps):
    mean = jnp.mean(values, axis=-1, keepdims=True)
    var = jnp.mean(values * values, axis=-1, keepdims=True) - mean * mean
    return (values - mean) * lax.rsqrt(var + eps)


def add_rows(left, piece):
    return jnp.dot(left, piece, preferred_element_type=jnp.float32)


def head_norm(values, gain, eps):
    rows, images, width = values.shape
    heads_here = width // HEAD_DIM
    shaped = values.reshape(rows, images, heads_here, HEAD_DIM)
    normed = layer_norm_rows(shaped, eps) * gain.reshape(heads_here, HEAD_DIM)
    return normed.astype(jnp.bfloat16).reshape(rows, images * heads_here, HEAD_DIM)


def shift_pairs(sx, sy):
    return [
        (x * RING + y, ((x + sx) % RING) * RING + (y + sy) % RING)
        for x in range(RING)
        for y in range(RING)
    ]


def near_pair(group, along_x):
    sx, sy = (1, 0) if along_x else (0, 1)
    from_minus = lax.ppermute(group, "tok", shift_pairs(sx, sy))
    from_plus = lax.ppermute(group, "tok", shift_pairs(-sx, -sy))
    return from_minus, from_plus


def far_block(from_minus, from_plus, along_x):
    sx, sy = (1, 0) if along_x else (0, 1)
    half = from_minus.shape[-1] // 2
    first = lax.ppermute(from_minus[..., :half], "tok", shift_pairs(sx, sy))
    second = lax.ppermute(from_plus[..., half:], "tok", shift_pairs(-sx, -sy))
    return jnp.concatenate([first, second], axis=-1)


def ring_project(rolled, blocks):
    half = blocks.shape[-1] // 2
    pieces = (blocks[..., :half], blocks[..., half:])
    inner_x = (False, True)
    near, far = [], []
    for h in (0, 1):
        near.append(near_pair(pieces[h], inner_x[h]))
    for h in (0, 1):
        far.append(far_block(*near[h], inner_x[h]))
    inner = [
        jnp.stack([pieces[h], near[h][1], far[h], near[h][0]], axis=1) for h in range(2)
    ]
    outer_near = []
    for h in (0, 1):
        outer_near.append(near_pair(inner[h], not inner_x[h]))
    outer_far = [far_block(*outer_near[h], not inner_x[h]) for h in range(2)]
    parts = []
    for h in range(2):
        got_all = [inner[h], outer_near[h][1], outer_far[h], outer_near[h][0]]
        total = None
        for k, got in enumerate(got_all):
            lhs = rolled[k] if h == 0 else rolled[:, k]
            term = jnp.einsum("btr,mbrc->mtc", lhs, got, preferred_element_type=jnp.float32)
            total = term if total is None else total + term
        parts.append(total)
    return jnp.concatenate(parts, axis=-1)


def roll_major(values):
    t = lax.axis_index("tok")
    out = values
    for axis, shift in ((0, t // RING), (1, t % RING)):
        doubled = jnp.concatenate([out, out], axis=axis)
        starts = [0] * out.ndim
        starts[axis] = shift
        out = lax.dynamic_slice(doubled, starts, out.shape)
    return out


def contract_blocks(blocks, weight):
    rows = blocks.shape[-1]
    shaped = weight.reshape(RING, RING, rows, weight.shape[-1])
    return jnp.einsum("abtr,abrc->tc", blocks, shaped, preferred_element_type=jnp.float32)


def local(patches, w_query, w_key, w_value, q_gain, k_gain, w_out):
    local_rows, images, local_width = patches.shape
    tokens = local_rows * images
    sub = D // (RING * RING)
    pieces = patches.reshape(tokens, local_width // sub, sub).transpose(1, 0, 2)
    whole_raw = lax.all_gather(pieces, "wid", axis=0, tiled=True).astype(jnp.float32)
    mean = jnp.mean(whole_raw, axis=(0, 2), keepdims=True)
    var = jnp.mean(whole_raw * whole_raw, axis=(0, 2), keepdims=True) - mean * mean
    normed = ((whole_raw - mean) * lax.rsqrt(var + 1e-06)).astype(jnp.bfloat16)
    normed = normed.reshape(RING, RING, tokens, sub)
    rolled = roll_major(normed)

    projected = ring_project(rolled, jnp.stack([w_query, w_key]))
    query = projected[0]
    key = projected[1]
    value = contract_blocks(normed, lax.all_gather(w_value, "tok", axis=0, tiled=True))
    head_width = query.shape[1]
    heads_here = head_width // HEAD_DIM
    qnorm = head_norm(query.reshape(local_rows, images, head_width), q_gain, 1e-06)
    knorm = head_norm(key.reshape(local_rows, images, head_width), k_gain, 1e-06)
    vshaped = value.astype(jnp.bfloat16).reshape(local_rows, images * heads_here, HEAD_DIM)
    vfull = lax.all_to_all(vshaped, "tok", split_axis=1, concat_axis=0, tiled=True)
    stacked = jnp.stack([qnorm, knorm], axis=1)
    spread = lax.all_to_all(stacked, "tok", split_axis=2, concat_axis=0, tiled=True)
    qfull, kfull = spread[:, 0], spread[:, 1]
    seq_rows, item_count, _ = qfull.shape
    block = seq_rows
    blocks = qfull.reshape(seq_rows // block, block, item_count, HEAD_DIM)
    scale = HEAD_DIM ** (-0.5)

    def attend(qblock):
        scores = (
            jnp.einsum("qid,kid->iqk", qblock, kfull, preferred_element_type=jnp.float32) * scale
        )
        top = jnp.max(scores, axis=-1, keepdims=True)
        expo = jnp.exp(scores - top)
        probs = (expo / jnp.sum(expo, axis=-1, keepdims=True)).astype(jnp.bfloat16)
        return jnp.einsum("iqk,kid->qid", probs, vfull, preferred_element_type=jnp.float32).astype(
            jnp.bfloat16
        )

    attended = lax.map(attend, blocks).reshape(seq_rows, item_count, HEAD_DIM)
    returned = lax.all_to_all(attended, "tok", split_axis=0, concat_axis=1, tiled=True)
    mixed = returned.reshape(local_rows, images, head_width)
    w_out_whole = lax.all_gather(w_out, "tok", axis=0, tiled=True)
    split = local_rows // 2
    results = []
    for rows in (slice(0, split), slice(split, local_rows)):
        piece = lax.all_gather(mixed[rows], "wid", axis=2, tiled=True)
        branch = add_rows(piece.reshape(-1, HD), w_out_whole)
        as_float = patches[rows].astype(jnp.float32)
        results.append((as_float + branch.reshape(as_float.shape)).astype(jnp.bfloat16))
    return jnp.concatenate(results, axis=0)


def solution(mesh):
    placed = (
        P("tok", None, "wid"),
        P("tok", "wid"),
        P("tok", "wid"),
        P("tok", "wid"),
        P("wid"),
        P("wid"),
        P("tok", "wid"),
    )

    return jax.shard_map(
        local, mesh=mesh, in_specs=placed, out_specs=P("tok", None, "wid"), check_vma=False
    )
```

```python
import jax
import jax.numpy as jnp
from jax import lax
from jax.sharding import PartitionSpec as P


D = 6144
HEAD_DIM = 128
HD = 4096
RING = 4


def layer_norm_rows(values, eps):
    mean = jnp.mean(values, axis=-1, keepdims=True)
    var = jnp.mean(values * values, axis=-1, keepdims=True) - mean * mean
    return (values - mean) * lax.rsqrt(var + eps)


def add_rows(left, piece):
    return jnp.dot(left, piece, preferred_element_type=jnp.float32)


def head_norm(values, gain, eps):
    rows, images, width = values.shape
    heads_here = width // HEAD_DIM
    shaped = values.reshape(rows, images, heads_here, HEAD_DIM)
    normed = layer_norm_rows(shaped, eps) * gain.reshape(heads_here, HEAD_DIM)
    return normed.astype(jnp.bfloat16).reshape(rows, images * heads_here, HEAD_DIM)


def shift_pairs(sx, sy):
    return [
        (x * RING + y, ((x + sx) % RING) * RING + (y + sy) % RING)
        for x in range(RING)
        for y in range(RING)
    ]


def near_pair(group, along_x):
    sx, sy = (1, 0) if along_x else (0, 1)
    from_minus = lax.ppermute(group, "tok", shift_pairs(sx, sy))
    from_plus = lax.ppermute(group, "tok", shift_pairs(-sx, -sy))
    return from_minus, from_plus


def far_block(from_minus, from_plus, along_x):
    sx, sy = (1, 0) if along_x else (0, 1)
    half = from_minus.shape[-1] // 2
    first = lax.ppermute(from_minus[..., :half], "tok", shift_pairs(sx, sy))
    second = lax.ppermute(from_plus[..., half:], "tok", shift_pairs(-sx, -sy))
    return jnp.concatenate([first, second], axis=-1)


def ring_project(rolled, blocks):
    half = blocks.shape[-1] // 2
    pieces = (blocks[..., :half], blocks[..., half:])
    inner_x = (False, True)
    near, far = [], []
    for h in (0, 1):
        near.append(near_pair(pieces[h], inner_x[h]))
    for h in (0, 1):
        far.append(far_block(*near[h], inner_x[h]))
    inner = [
        jnp.stack([pieces[h], near[h][1], far[h], near[h][0]], axis=1) for h in range(2)
    ]
    outer_near = []
    for h in (0, 1):
        outer_near.append(near_pair(inner[h], not inner_x[h]))
    outer_far = [far_block(*outer_near[h], not inner_x[h]) for h in range(2)]
    parts = []
    for h in range(2):
        got_all = [inner[h], outer_near[h][1], outer_far[h], outer_near[h][0]]
        total = None
        for k, got in enumerate(got_all):
            lhs = rolled[k] if h == 0 else rolled[:, k]
            term = jnp.einsum("btr,mbrc->mtc", lhs, got, preferred_element_type=jnp.float32)
            total = term if total is None else total + term
        parts.append(total)
    return jnp.concatenate(parts, axis=-1)


def roll_major(values):
    t = lax.axis_index("tok")
    out = values
    for axis, shift in ((0, t // RING), (1, t % RING)):
        doubled = jnp.concatenate([out, out], axis=axis)
        starts = [0] * out.ndim
        starts[axis] = shift
        out = lax.dynamic_slice(doubled, starts, out.shape)
    return out


def contract_blocks(blocks, weight):
    rows = blocks.shape[-1]
    shaped = weight.reshape(RING, RING, rows, weight.shape[-1])
    return jnp.einsum("abtr,abrc->tc", blocks, shaped, preferred_element_type=jnp.float32)


def local(patches, w_query, w_key, w_value, q_gain, k_gain, w_out):
    local_rows, images, local_width = patches.shape
    tokens = local_rows * images
    sub = D // (RING * RING)
    pieces = patches.reshape(tokens, local_width // sub, sub).transpose(1, 0, 2)
    whole_raw = lax.all_gather(pieces, "wid", axis=0, tiled=True).astype(jnp.float32)
    mean = jnp.mean(whole_raw, axis=(0, 2), keepdims=True)
    var = jnp.mean(whole_raw * whole_raw, axis=(0, 2), keepdims=True) - mean * mean
    normed = ((whole_raw - mean) * lax.rsqrt(var + 1e-06)).astype(jnp.bfloat16)
    normed = normed.reshape(RING, RING, tokens, sub)
    rolled = roll_major(normed)

    projected = ring_project(rolled, jnp.stack([w_query, w_key]))
    query = projected[0]
    key = projected[1]
    value = contract_blocks(normed, lax.all_gather(w_value, "tok", axis=0, tiled=True))
    head_width = query.shape[1]
    heads_here = head_width // HEAD_DIM
    qnorm = head_norm(query.reshape(local_rows, images, head_width), q_gain, 1e-06)
    knorm = head_norm(key.reshape(local_rows, images, head_width), k_gain, 1e-06)
    vshaped = value.astype(jnp.bfloat16).reshape(local_rows, images * heads_here, HEAD_DIM)
    vfull = lax.all_to_all(vshaped, "tok", split_axis=1, concat_axis=0, tiled=True)
    stacked = jnp.stack([qnorm, knorm], axis=1)
    spread = lax.all_to_all(stacked, "tok", split_axis=2, concat_axis=0, tiled=True)
    qfull, kfull = spread[:, 0], spread[:, 1]
    seq_rows, item_count, _ = qfull.shape
    block = seq_rows
    blocks = qfull.reshape(seq_rows // block, block, item_count, HEAD_DIM)
    scale = HEAD_DIM ** (-0.5)

    def attend(qblock):
        scores = (
            jnp.einsum("qid,kid->iqk", qblock, kfull, preferred_element_type=jnp.float32) * scale
        )
        top = jnp.max(scores, axis=-1, keepdims=True)
        expo = jnp.exp(scores - top)
        probs = (expo / jnp.sum(expo, axis=-1, keepdims=True)).astype(jnp.bfloat16)
        return jnp.einsum("iqk,kid->qid", probs, vfull, preferred_element_type=jnp.float32).astype(
            jnp.bfloat16
        )

    attended = lax.map(attend, blocks).reshape(seq_rows, item_count, HEAD_DIM)
    returned = lax.all_to_all(attended, "tok", split_axis=0, concat_axis=1, tiled=True)
    mixed = returned.reshape(local_rows, images, head_width)
    mixed_whole = lax.all_gather(mixed, "wid", axis=2, tiled=True).reshape(tokens, HD)
    branch = add_rows(mixed_whole, lax.all_gather(w_out, "tok", axis=0, tiled=True))
    as_float = patches.astype(jnp.float32)
    return (as_float + branch.reshape(local_rows, images, local_width)).astype(jnp.bfloat16)


def solution(mesh):
    placed = (
        P("tok", None, "wid"),
        P("tok", "wid"),
        P("tok", "wid"),
        P("tok", "wid"),
        P("wid"),
        P("wid"),
        P("tok", "wid"),
    )

    return jax.shard_map(
        local, mesh=mesh, in_specs=placed, out_specs=P("tok", None, "wid"), check_vma=False
    )
```
